256 devices in a mesh: dp: 8 (over y, core), expert: 32 (over x, z).
Axes of the slice: x: 4, y: 4, z: 8, core: 2. Of those that a mesh axis runs over, the one named last changes fastest.
Arguments:
- tokens: bfloat16 [32768, 2048], P(('dp', 'expert')), may hold values from -6 to 6
- tangents: bfloat16 [32768, 2048], P(('dp', 'expert')), may hold values from -6 to 6
- cotangents: bfloat16 [32768, 2048], P(('dp', 'expert')), may hold values from -6 to 6
- routes: int32 [32768, 2], P(('dp', 'expert')), may hold values from 0 to 31, all different within a row; in each aligned block of 128 rows (0 to 127, 128 to 255, ...) at most 16 rows name the same one
- gates: bfloat16 [32768, 2], P(('dp', 'expert')), may hold values from 0.19921875 to 1
- w_up: bfloat16 [32, 2048, 768], P('expert'), may hold values from -0.125 to 0.125
- w_down: bfloat16 [32, 768, 2048], P('expert'), may hold values from -0.21875 to 0.21875
- v_up: bfloat16 [32, 2048, 768], P('expert'), may hold values from -0.125 to 0.125
Outputs:
- hvp_tokens: bfloat16 [32768, 2048], P(('dp', 'expert'))
- hvp_up: bfloat16 [32, 2048, 768], P('expert', 'dp')
- hvp_down: bfloat16 [32, 768, 2048], P('expert', None, 'dp')
The draws below stay inside these ranges and needn't reach their ends.
Inputs may be any that keep to these rules, and one draw needn't show every extreme that they name: `routes`: A token's 2 experts differ. Among the 128 tokens of one device no expert is named more than 16 times, and in every draw some device names some expert exactly 16 times.
All inputs are finite; a program needn't handle non-finite values.
Results may differ from the reference program's by a relative error of at most 0.014.
Values may be sent and summed in bfloat16 or wider, within the bound.
No kernel may reach another device: no remote copies, remote signals or barrier semaphores. Data moves between devices by JAX's collectives and lax.ppermute only.
A program may use at most 128 MiB of HBM per device.

```python
import math
import jax
import jax.numpy as jnp
import numpy as np
from jax import lax

D = 2048
FF = 768
TOK_DEV = 128
TOP = 2
EXPERTS = 32
CAP = 16
TOKENS = 32768
N_DP = 8
N_EXPERT = 32


def block_scale(stream_key, extent, pieces, low, largest):
    factor_of, own = 1.0, jax.random.fold_in(stream_key, 6)
    for position, parts in pieces:
        draws = jnp.exp(jax.random.uniform(jax.random.fold_in(own, position), (parts,), jnp.float32, low / len(pieces), largest / len(pieces)))
        factor_of = factor_of * jnp.repeat(draws, extent[position] // parts).reshape([-1 if axis == position else 1 for axis in range(len(extent))])
    return factor_of


def assign_block(key, own, number, rows, amount, top, most, skew):
    ranking = jax.random.permutation(key, amount)
    packed, ordinary = portions_of(amount, rows * top, most, skew, True), portions_of(amount, rows * top, most, skew, False)
    places = jnp.arange(amount)

    def named(lengths, offset_by):
        used = int((lengths > 0).sum())
        fixed = max(1, used // 4)
        shifted = fixed + (places - fixed + offset_by * (used - fixed)) % max(1, amount - fixed)
        return jnp.zeros((amount,), jnp.int32).at[ranking[jnp.where(places < fixed, places, shifted)]].set(jnp.asarray(lengths, jnp.int32))

    lengths = jnp.where(number % 4 == 0, named(packed, number // 4), named(ordinary, number - number // 4 - 1))
    mixed = jax.random.permutation(jax.random.fold_in(own, 3), amount)
    donor, receiver = mixed[0:amount // 2 * 2:2], mixed[1:amount // 2 * 2:2]
    margin = jnp.minimum(lengths[donor] - 1, most - lengths[receiver]) // 2
    margin = jnp.where((donor == ranking[0]) | (receiver == ranking[0]) | (lengths[receiver] == 0), 0, jnp.maximum(margin, 0))
    shifted = jax.random.randint(jax.random.fold_in(own, 4), (amount // 2,), 0, 1 << 20) % (margin + 1)
    lengths = lengths.at[donor].add(-shifted).at[receiver].add(shifted)
    labels = jnp.searchsorted(jnp.cumsum(lengths), jnp.arange(rows * top), side="right").astype(jnp.int32)
    table = labels.reshape(top, rows).T
    table = table[jax.random.permutation(jax.random.fold_in(own, 1), rows)]
    offset_by = jax.random.randint(jax.random.fold_in(own, 2), (rows, 1), 0, top)
    return jnp.take_along_axis(table, (jnp.arange(top)[None, :] + offset_by) % top, axis=1)


def portions_of(amount, total, reach, skew, full):
    loads = [(1 << 20) // math.isqrt(standing ** skew) + 1 for standing in range(1, amount + 1)]
    largest = reach if full else min(reach, max(-(-total // amount), total * loads[0] // sum(loads)))
    least = 1 if total - largest >= amount - 1 else 0
    given, rest = [largest] + [least] * (amount - 1), total - largest - least * (amount - 1)
    while rest > 0:
        free = [i for i in range(1, amount) if given[i] < largest] or [i for i in range(1, amount) if given[i] < reach]
        whole, budget = sum([loads[i] for i in free]), rest
        for i in free:
            addition = min(reach - given[i], max(1, budget * loads[i] // whole), rest)
            given[i] = given[i] + addition
            rest = rest - addition
    return np.array(given)


def scatter_about(key, dims, width, most, split=(), held_as=jnp.bfloat16):
    values = jax.random.normal(key, dims, jnp.float32) * width
    if len(split) > 0:
        values = block_scale(key, dims, split, -0.22, 0.18) * values
    return jnp.clip(values, min=-most, max=most).astype(held_as)


def setup_inputs(seed: int = 0) -> dict:
    streams_of = jax.random.split(jax.random.key(seed), 9)
    tokens = scatter_about(streams_of[0], (TOKENS, D), 1.0, 6.0, ((0, 256),))
    tangents = scatter_about(streams_of[1], (TOKENS, D), 1.0, 6.0, ((0, 256),))
    cotangents = scatter_about(streams_of[2], (TOKENS, D), 1.0, 6.0, ((0, 256),))
    routes_keys = jax.random.split(jax.random.fold_in(streams_of[3], 1), TOKENS // TOK_DEV)
    routes_turns = jax.random.permutation(jax.random.fold_in(streams_of[3], 3), TOKENS // TOK_DEV)
    routes = jax.vmap(lambda own, number: assign_block(jax.random.fold_in(streams_of[3], 2), own, number, TOK_DEV, EXPERTS, TOP, CAP, 2))(routes_keys, routes_turns).reshape((TOKENS, TOP))
    gates = jnp.clip(0.19921875 + 0.80078125 * jax.random.uniform(streams_of[4], (TOKENS, TOP), jnp.float32) ** block_scale(streams_of[4], (TOKENS, TOP), ((0, 256),), -0.2, 0.2), 0.19921875, 1.0).astype(jnp.bfloat16)
    w_up = scatter_about(streams_of[5], (EXPERTS, D, FF), D ** -0.5, 0.125, ((0, 32),))
    w_down = scatter_about(streams_of[6], (EXPERTS, FF, D), FF ** -0.5, 0.21875, ((0, 32),))
    v_up = scatter_about(streams_of[7], (EXPERTS, D, FF), D ** -0.5, 0.125, ((0, 32),))
    return dict(tokens=tokens, tangents=tangents, cotangents=cotangents, routes=routes, gates=gates, w_up=w_up, w_down=w_down, v_up=v_up)


def slot_table(route_ids, expert_count, capacity):
    token_count, route_count = route_ids.shape
    flat_ids = route_ids.reshape(token_count * route_count)
    onehot = (flat_ids[:, None] == jnp.arange(expert_count, dtype=jnp.int32)[None, :]).astype(jnp.int32)
    before = jnp.cumsum(onehot, axis=0) - onehot
    slot_rank = lax.optimization_barrier(jnp.sum(before * onehot, axis=1))
    target = flat_ids * capacity + slot_rank
    slot_owner = jnp.full((expert_count * capacity,), -1, jnp.int32).at[target].set(jnp.arange(token_count * route_count, dtype=jnp.int32))
    return (target, slot_owner)

def gather_slots(rows, slot_owner, route_count):
    valid = slot_owner >= 0
    safe = jnp.where(valid, slot_owner, 0) // route_count
    picked = jnp.take(rows, safe, axis=0)
    return jnp.where(valid[:, None], picked, jnp.zeros_like(picked))

def gather_gates(gate_rows, slot_owner):
    valid = slot_owner >= 0
    flat_gate = gate_rows.reshape(-1)
    picked = jnp.take(flat_gate, jnp.where(valid, slot_owner, 0), axis=0)
    return jnp.where(valid, picked, jnp.zeros_like(picked))

def expert_terms(primal, tangent, cotan, gate_slot, up_proj, down_proj, dir_up):
    pre_act = jnp.dot(primal, up_proj, preferred_element_type=jnp.float32)
    pre_tan = jnp.dot(tangent, up_proj, preferred_element_type=jnp.float32) + jnp.dot(primal, dir_up, preferred_element_type=jnp.float32)
    sigmoid_z = jax.nn.sigmoid(pre_act)
    first_der = sigmoid_z * (1.0 + pre_act * (1.0 - sigmoid_z))
    second_der = sigmoid_z * (1.0 - sigmoid_z) * (2.0 + pre_act * (1.0 - 2.0 * sigmoid_z))
    hidden_tan = (first_der * pre_tan).astype(jnp.bfloat16)
    scaled_cot = (gate_slot.astype(jnp.float32)[:, None] * cotan.astype(jnp.float32)).astype(jnp.bfloat16)
    back_hid = jnp.dot(scaled_cot, down_proj.T, preferred_element_type=jnp.float32)
    back_pre = (back_hid * first_der).astype(jnp.bfloat16)
    back_tan = (back_hid * second_der * pre_tan).astype(jnp.bfloat16)
    input_hvp = (jnp.dot(back_tan, up_proj.T, preferred_element_type=jnp.float32) + jnp.dot(back_pre, dir_up.T, preferred_element_type=jnp.float32)).astype(jnp.bfloat16)
    hvp_first = jnp.dot(tangent.T, back_pre, preferred_element_type=jnp.float32) + jnp.dot(primal.T, back_tan, preferred_element_type=jnp.float32)
    hvp_second = jnp.dot(scaled_cot.T, hidden_tan, preferred_element_type=jnp.float32)
    return (input_hvp, hvp_first, hvp_second)

def reference(tokens, tangents, cotangents, routes, gates, w_up, w_down, v_up):
    blocks = N_DP * N_EXPERT
    tok_blocks = tokens.reshape(blocks, TOK_DEV, D)
    tan_blocks = tangents.reshape(blocks, TOK_DEV, D)
    cot_blocks = cotangents.reshape(blocks, TOK_DEV, D)
    route_blocks = routes.reshape(blocks, TOK_DEV, TOP)
    gate_blocks = gates.reshape(blocks, TOK_DEV * TOP)
    targets, owners = jax.vmap(lambda r: slot_table(r, EXPERTS, CAP))(route_blocks)
    scale = 1.0 / math.sqrt(TOK_DEV * TOP * N_DP)
    block_ids = jnp.arange(blocks, dtype=jnp.int32)[:, None]

    def one_expert(carry, expert_id):
        own = lax.dynamic_slice_in_dim(owners, expert_id * CAP, CAP, 1)
        gather_all = jax.vmap(lambda rows, o: gather_slots(rows, o, TOP))
        primal = gather_all(tok_blocks, own).reshape(N_DP, N_EXPERT * CAP, D)
        tangent = gather_all(tan_blocks, own).reshape(N_DP, N_EXPERT * CAP, D)
        cotan = gather_all(cot_blocks, own).reshape(N_DP, N_EXPERT * CAP, D)
        gate_slot = jax.vmap(gather_gates)(gate_blocks, own).reshape(N_DP, N_EXPERT * CAP)
        up_proj = w_up[expert_id]
        down_proj = w_down[expert_id]
        dir_up = v_up[expert_id]
        input_hvp, hvp_first, hvp_second = lax.map(lambda a: expert_terms(a[0], a[1], a[2], a[3], up_proj, down_proj, dir_up), (primal, tangent, cotan, gate_slot))
        first_parts = lax.optimization_barrier((hvp_first * scale).astype(jnp.bfloat16))
        second_parts = lax.optimization_barrier((hvp_second * scale).astype(jnp.bfloat16))
        sum_first = lax.optimization_barrier(jnp.sum(first_parts.astype(jnp.float32), axis=0)).astype(jnp.bfloat16)
        sum_second = lax.optimization_barrier(jnp.sum(second_parts.astype(jnp.float32), axis=0)).T.astype(jnp.bfloat16)
        valid = own >= 0
        token_ids = jnp.where(valid, own, 0) // TOP
        rows_back = input_hvp.reshape(blocks, CAP, D).astype(jnp.float32)
        rows_back = jnp.where(valid[:, :, None], rows_back, jnp.zeros_like(rows_back))
        carry = carry.at[jnp.broadcast_to(block_ids, token_ids.shape), token_ids].add(rows_back)
        return (carry, (sum_first, sum_second))
    start = jnp.zeros((blocks, TOK_DEV, D), jnp.float32)
    total, (hvp_up, hvp_down) = lax.scan(one_expert, start, jnp.arange(EXPERTS, dtype=jnp.int32))
    hvp_tokens = total.reshape(TOKENS, D).astype(jnp.bfloat16)
    return (hvp_tokens, hvp_up, hvp_down)
```

```python
import math

import jax
import jax.numpy as jnp
from jax import lax
from jax.sharding import PartitionSpec as P


def slot_matrices(route_ids, gate_rows, expert_count, capacity):
    token_count, route_count = route_ids.shape
    routes_total = token_count * route_count
    slots = expert_count * capacity
    flat_ids = route_ids.reshape(routes_total)
    onehot = (flat_ids[:, None] == jnp.arange(expert_count, dtype=jnp.int32)[None, :]).astype(
        jnp.bfloat16
    )
    order = jnp.arange(routes_total, dtype=jnp.int32)
    earlier = (order[None, :] < order[:, None]).astype(jnp.bfloat16)
    before = jnp.dot(earlier, onehot, preferred_element_type=jnp.float32)
    slot_rank = jnp.sum(before * onehot.astype(jnp.float32), axis=1).astype(jnp.int32)
    target = (flat_ids * capacity + slot_rank).reshape(token_count, route_count)
    slot_ids = jnp.arange(slots, dtype=jnp.int32)
    hit = target[:, :, None] == slot_ids[None, None, :]
    pick = jnp.any(hit, axis=1).astype(jnp.bfloat16)
    gate_pick = jnp.sum(
        jnp.where(hit, gate_rows.astype(jnp.float32)[:, :, None], 0.0), axis=1
    ).astype(jnp.bfloat16)
    return pick, gate_pick


def to_slots(pick, rows):
    return lax.dot_general(
        pick, rows, (((0,), (0,)), ((), ())), preferred_element_type=jnp.float32
    ).astype(jnp.bfloat16)


def per_device(tokens, tangents, cotangents, routes, gates, w_up, w_down, v_up):
    token_count, width = tokens.shape
    route_count = routes.shape[1]
    expert_count = lax.axis_size("expert")
    replicas = lax.axis_size("dp")
    capacity = max(2, token_count * route_count * 2 // expert_count)
    scale = 1.0 / math.sqrt(token_count * route_count * replicas)
    slots = expert_count * capacity
    pick, gate_pick = slot_matrices(routes, gates, expert_count, capacity)
    send_xt = jnp.concatenate([to_slots(pick, tokens), to_slots(pick, tangents)], axis=1)
    send_cot = to_slots(gate_pick, cotangents)
    recv_xt = lax.all_to_all(
        send_xt.reshape(expert_count, capacity, 2 * width),
        "expert",
        split_axis=0,
        concat_axis=0,
        tiled=True,
    ).reshape(slots, 2 * width)
    scaled_cot = lax.all_to_all(
        send_cot.reshape(expert_count, capacity, width),
        "expert",
        split_axis=0,
        concat_axis=0,
        tiled=True,
    ).reshape(slots, width)
    primal = recv_xt[:, :width]
    tangent = recv_xt[:, width:]
    up_proj = w_up[0]
    down_proj = w_down[0]
    dir_up = v_up[0]
    pre_act = jnp.dot(primal, up_proj, preferred_element_type=jnp.float32)
    pre_tan = jnp.dot(tangent, up_proj, preferred_element_type=jnp.float32) + jnp.dot(
        primal, dir_up, preferred_element_type=jnp.float32
    )
    sigmoid_z = jax.nn.sigmoid(pre_act)
    first_der = sigmoid_z * (1.0 + pre_act * (1.0 - sigmoid_z))
    second_der = sigmoid_z * (1.0 - sigmoid_z) * (2.0 + pre_act * (1.0 - 2.0 * sigmoid_z))
    hidden_tan = (first_der * pre_tan).astype(jnp.bfloat16)
    back_hid = jnp.dot(scaled_cot, down_proj.T, preferred_element_type=jnp.float32)
    back_pre = (back_hid * first_der).astype(jnp.bfloat16)
    back_tan = (back_hid * second_der * pre_tan).astype(jnp.bfloat16)
    input_hvp = (
        jnp.dot(back_tan, up_proj.T, preferred_element_type=jnp.float32)
        + jnp.dot(back_pre, dir_up.T, preferred_element_type=jnp.float32)
    ).astype(jnp.bfloat16)
    returned = lax.all_to_all(
        input_hvp.reshape(expert_count, capacity, width),
        "expert",
        split_axis=0,
        concat_axis=0,
        tiled=True,
    ).reshape(slots, width)
    hvp_tokens = jnp.dot(pick, returned, preferred_element_type=jnp.float32).astype(jnp.bfloat16)
    first = jnp.dot(tangent.T, back_pre, preferred_element_type=jnp.float32) + jnp.dot(
        primal.T, back_tan, preferred_element_type=jnp.float32
    )
    second = jnp.dot(scaled_cot.T, hidden_tan, preferred_element_type=jnp.float32)
    summed = lax.psum_scatter(
        (jnp.concatenate([first, second], axis=1) * scale).astype(jnp.bfloat16),
        "dp",
        scatter_dimension=0,
        tiled=True,
    ).astype(jnp.float32)
    hidden_units = up_proj.shape[1]
    hvp_up = summed[:, :hidden_units].astype(jnp.bfloat16)[None]
    hvp_down = summed[:, hidden_units:].T.astype(jnp.bfloat16)[None]
    return (hvp_tokens, hvp_up, hvp_down)


def solution(mesh):
    in_specs = (
        P(("dp", "expert"), None),
        P(("dp", "expert"), None),
        P(("dp", "expert"), None),
        P(("dp", "expert"), None),
        P(("dp", "expert"), None),
        P("expert", None, None),
        P("expert", None, None),
        P("expert", None, None),
    )
    out_specs = (P(("dp", "expert"), None), P("expert", "dp", None), P("expert", None, "dp"))
    return jax.shard_map(
        per_device, mesh=mesh, in_specs=in_specs, out_specs=out_specs, check_vma=False
    )
```

```python
import math

import jax
import jax.numpy as jnp
from jax import lax
from jax.sharding import PartitionSpec as P


def slot_matrices(route_ids, gate_rows, expert_count, capacity):
    token_count, route_count = route_ids.shape
    routes_total = token_count * route_count
    slots = expert_count * capacity
    flat_ids = route_ids.reshape(routes_total)
    onehot = (flat_ids[:, None] == jnp.arange(expert_count, dtype=jnp.int32)[None, :]).astype(
        jnp.bfloat16
    )
    order = jnp.arange(routes_total, dtype=jnp.int32)
    earlier = (order[None, :] < order[:, None]).astype(jnp.bfloat16)
    before = jnp.dot(earlier, onehot, preferred_element_type=jnp.float32)
    slot_rank = jnp.sum(before * onehot.astype(jnp.float32), axis=1).astype(jnp.int32)
    target = (flat_ids * capacity + slot_rank).reshape(token_count, route_count)
    slot_ids = jnp.arange(slots, dtype=jnp.int32)
    hit = target[:, :, None] == slot_ids[None, None, :]
    pick = jnp.any(hit, axis=1).astype(jnp.bfloat16)
    gate_pick = jnp.sum(
        jnp.where(hit, gate_rows.astype(jnp.float32)[:, :, None], 0.0), axis=1
    ).astype(jnp.bfloat16)
    return pick, gate_pick


def to_slots(pick, rows):
    return lax.dot_general(
        pick, rows, (((0,), (0,)), ((), ())), preferred_element_type=jnp.float32
    ).astype(jnp.bfloat16)


def per_device(tokens, tangents, cotangents, routes, gates, w_up, w_down, v_up):
    token_count, width = tokens.shape
    route_count = routes.shape[1]
    expert_count = lax.axis_size("expert")
    replicas = lax.axis_size("dp")
    capacity = max(2, token_count * route_count * 2 // expert_count)
    scale = 1.0 / math.sqrt(token_count * route_count * replicas)
    slots = expert_count * capacity
    pick, gate_pick = slot_matrices(routes, gates, expert_count, capacity)
    send_xt = jnp.concatenate([to_slots(pick, tokens), to_slots(pick, tangents)], axis=1)
    send_cot = to_slots(gate_pick, cotangents)
    recv_xt = lax.all_to_all(
        send_xt.reshape(expert_count, capacity, 2 * width),
        "expert",
        split_axis=0,
        concat_axis=0,
        tiled=True,
    ).reshape(slots, 2 * width)
    recv_xt, send_cot = lax.optimization_barrier((recv_xt, send_cot))
    scaled_cot = lax.all_to_all(
        send_cot.reshape(expert_count, capacity, width),
        "expert",
        split_axis=0,
        concat_axis=0,
        tiled=True,
    ).reshape(slots, width)
    primal = recv_xt[:, :width]
    tangent = recv_xt[:, width:]
    up_proj = w_up[0]
    down_proj = w_down[0]
    dir_up = v_up[0]
    pre_act = jnp.dot(primal, up_proj, preferred_element_type=jnp.float32)
    pre_tan = jnp.dot(tangent, up_proj, preferred_element_type=jnp.float32) + jnp.dot(
        primal, dir_up, preferred_element_type=jnp.float32
    )
    sigmoid_z = jax.nn.sigmoid(pre_act)
    first_der = sigmoid_z * (1.0 + pre_act * (1.0 - sigmoid_z))
    second_der = sigmoid_z * (1.0 - sigmoid_z) * (2.0 + pre_act * (1.0 - 2.0 * sigmoid_z))
    hidden_tan = (first_der * pre_tan).astype(jnp.bfloat16)
    back_hid = jnp.dot(scaled_cot, down_proj.T, preferred_element_type=jnp.float32)
    back_pre = (back_hid * first_der).astype(jnp.bfloat16)
    back_tan = (back_hid * second_der * pre_tan).astype(jnp.bfloat16)
    second = jnp.dot(scaled_cot.T, hidden_tan, preferred_element_type=jnp.float32)
    down_sum = lax.psum_scatter(
        (second * scale).astype(jnp.bfloat16), "dp", scatter_dimension=0, tiled=True
    )
    input_hvp = (
        jnp.dot(back_tan, up_proj.T, preferred_element_type=jnp.float32)
        + jnp.dot(back_pre, dir_up.T, preferred_element_type=jnp.float32)
    ).astype(jnp.bfloat16)
    returned = lax.all_to_all(
        input_hvp.reshape(expert_count, capacity, width),
        "expert",
        split_axis=0,
        concat_axis=0,
        tiled=True,
    ).reshape(slots, width)
    hvp_tokens = jnp.dot(pick, returned, preferred_element_type=jnp.float32).astype(jnp.bfloat16)
    first = jnp.dot(tangent.T, back_pre, preferred_element_type=jnp.float32) + jnp.dot(
        primal.T, back_tan, preferred_element_type=jnp.float32
    )
    up_sum = lax.psum_scatter(
        (first * scale).astype(jnp.bfloat16), "dp", scatter_dimension=0, tiled=True
    )
    hvp_up = up_sum[None]
    hvp_down = down_sum.T[None]
    return (hvp_tokens, hvp_up, hvp_down)


def solution(mesh):
    in_specs = (
        P(("dp", "expert"), None),
        P(("dp", "expert"), None),
        P(("dp", "expert"), None),
        P(("dp", "expert"), None),
        P(("dp", "expert"), None),
        P("expert", None, None),
        P("expert", None, None),
        P("expert", None, None),
    )
    out_specs = (P(("dp", "expert"), None), P("expert", "dp", None), P("expert", None, "dp"))
    return jax.shard_map(
        per_device, mesh=mesh, in_specs=in_specs, out_specs=out_specs, check_vma=False
    )
```

```python
import math

import jax
import jax.numpy as jnp
from jax import lax
from jax.sharding import PartitionSpec as P


def slot_matrices(route_ids, gate_rows, expert_count, capacity):
    token_count, route_count = route_ids.shape
    routes_total = token_count * route_count
    slots = expert_count * capacity
    flat_ids = route_ids.reshape(routes_total)
    onehot = (flat_ids[:, None] == jnp.arange(expert_count, dtype=jnp.int32)[None, :]).astype(
        jnp.bfloat16
    )
    order = jnp.arange(routes_total, dtype=jnp.int32)
    earlier = (order[None, :] < order[:, None]).astype(jnp.bfloat16)
    before = jnp.dot(earlier, onehot, preferred_element_type=jnp.float32)
    slot_rank = jnp.sum(before * onehot.astype(jnp.float32), axis=1).astype(jnp.int32)
    target = (flat_ids * capacity + slot_rank).reshape(token_count, route_count)
    slot_ids = jnp.arange(slots, dtype=jnp.int32)
    hit = target[:, :, None] == slot_ids[None, None, :]
    pick = jnp.any(hit, axis=1).astype(jnp.bfloat16)
    gate_pick = jnp.sum(
        jnp.where(hit, gate_rows.astype(jnp.float32)[:, :, None], 0.0), axis=1
    ).astype(jnp.bfloat16)
    return pick, gate_pick


def to_slots(pick, rows):
    return lax.dot_general(
        pick, rows, (((0,), (0,)), ((), ())), preferred_element_type=jnp.float32
    ).astype(jnp.bfloat16)


def per_device(tokens, tangents, cotangents, routes, gates, w_up, w_down, v_up):
    token_count, width = tokens.shape
    route_count = routes.shape[1]
    expert_count = lax.axis_size("expert")
    replicas = lax.axis_size("dp")
    capacity = max(2, token_count * route_count * 2 // expert_count)
    scale = 1.0 / math.sqrt(token_count * route_count * replicas)
    slots = expert_count * capacity
    pick, gate_pick = slot_matrices(routes, gates, expert_count, capacity)
    send_xg = jnp.concatenate([to_slots(pick, tokens), to_slots(gate_pick, cotangents)], axis=1)
    send_tan = to_slots(pick, tangents)
    recv_xg = lax.all_to_all(
        send_xg.reshape(expert_count, capacity, 2 * width),
        "expert",
        split_axis=0,
        concat_axis=0,
        tiled=True,
    ).reshape(slots, 2 * width)
    recv_xg, send_tan = lax.optimization_barrier((recv_xg, send_tan))
    tangent = lax.all_to_all(
        send_tan.reshape(expert_count, capacity, width),
        "expert",
        split_axis=0,
        concat_axis=0,
        tiled=True,
    ).reshape(slots, width)
    primal = recv_xg[:, :width]
    scaled_cot = recv_xg[:, width:]
    up_proj = w_up[0]
    down_proj = w_down[0]
    dir_up = v_up[0]
    pre_act = jnp.dot(primal, up_proj, preferred_element_type=jnp.float32)
    sigmoid_z = jax.nn.sigmoid(pre_act)
    first_der = sigmoid_z * (1.0 + pre_act * (1.0 - sigmoid_z))
    second_der = sigmoid_z * (1.0 - sigmoid_z) * (2.0 + pre_act * (1.0 - 2.0 * sigmoid_z))
    back_hid = jnp.dot(scaled_cot, down_proj.T, preferred_element_type=jnp.float32)
    back_pre = (back_hid * first_der).astype(jnp.bfloat16)
    pre_mix = jnp.dot(primal, dir_up, preferred_element_type=jnp.float32)
    hvp_mix = jnp.dot(back_pre, dir_up.T, preferred_element_type=jnp.float32)
    pre_tan = jnp.dot(tangent, up_proj, preferred_element_type=jnp.float32) + pre_mix
    hidden_tan = (first_der * pre_tan).astype(jnp.bfloat16)
    back_tan = (back_hid * second_der * pre_tan).astype(jnp.bfloat16)
    input_hvp = (jnp.dot(back_tan, up_proj.T, preferred_element_type=jnp.float32) + hvp_mix).astype(
        jnp.bfloat16
    )
    returned = lax.all_to_all(
        input_hvp.reshape(expert_count, capacity, width),
        "expert",
        split_axis=0,
        concat_axis=0,
        tiled=True,
    ).reshape(slots, width)
    second = jnp.dot(scaled_cot.T, hidden_tan, preferred_element_type=jnp.float32)
    down_sum = lax.psum_scatter(
        (second * scale).astype(jnp.bfloat16), "dp", scatter_dimension=0, tiled=True
    )
    hvp_tokens = jnp.dot(pick, returned, preferred_element_type=jnp.float32).astype(jnp.bfloat16)
    first = jnp.dot(tangent.T, back_pre, preferred_element_type=jnp.float32) + jnp.dot(
        primal.T, back_tan, preferred_element_type=jnp.float32
    )
    up_sum = lax.psum_scatter(
        (first * scale).astype(jnp.bfloat16), "dp", scatter_dimension=0, tiled=True
    )
    hvp_up = up_sum[None]
    hvp_down = down_sum.T[None]
    return (hvp_tokens, hvp_up, hvp_down)


def solution(mesh):
    in_specs = (
        P(("dp", "expert"), None),
        P(("dp", "expert"), None),
        P(("dp", "expert"), None),
        P(("dp", "expert"), None),
        P(("dp", "expert"), None),
        P("expert", None, None),
        P("expert", None, None),
        P("expert", None, None),
    )
    out_specs = (P(("dp", "expert"), None), P("expert", "dp", None), P("expert", None, "dp"))
    return jax.shard_map(
        per_device, mesh=mesh, in_specs=in_specs, out_specs=out_specs, check_vma=False
    )
```

```python
import math

import jax
import jax.numpy as jnp
from jax import lax
from jax.sharding import PartitionSpec as P


def slot_matrices(route_ids, gate_rows, expert_count, capacity):
    token_count, route_count = route_ids.shape
    routes_total = token_count * route_count
    slots = expert_count * capacity
    flat_ids = route_ids.reshape(routes_total)
    onehot = (flat_ids[:, None] == jnp.arange(expert_count, dtype=jnp.int32)[None, :]).astype(
        jnp.bfloat16
    )
    order = jnp.arange(routes_total, dtype=jnp.int32)
    earlier = (order[None, :] < order[:, None]).astype(jnp.bfloat16)
    before = jnp.dot(earlier, onehot, preferred_element_type=jnp.float32)
    slot_rank = jnp.sum(before * onehot.astype(jnp.float32), axis=1).astype(jnp.int32)
    target = (flat_ids * capacity + slot_rank).reshape(token_count, route_count)
    slot_ids = jnp.arange(slots, dtype=jnp.int32)
    hit = target[:, :, None] == slot_ids[None, None, :]
    pick = jnp.any(hit, axis=1).astype(jnp.bfloat16)
    gate_pick = jnp.sum(
        jnp.where(hit, gate_rows.astype(jnp.float32)[:, :, None], 0.0), axis=1
    ).astype(jnp.bfloat16)
    return pick, gate_pick


def to_slots(pick, rows):
    return lax.dot_general(
        pick, rows, (((0,), (0,)), ((), ())), preferred_element_type=jnp.float32
    ).astype(jnp.bfloat16)


def per_device(tokens, tangents, cotangents, routes, gates, w_up, w_down, v_up):
    token_count, width = tokens.shape
    route_count = routes.shape[1]
    expert_count = lax.axis_size("expert")
    replicas = lax.axis_size("dp")
    capacity = max(2, token_count * route_count * 2 // expert_count)
    scale = 1.0 / math.sqrt(token_count * route_count * replicas)
    slots = expert_count * capacity
    pick, gate_pick = slot_matrices(routes, gates, expert_count, capacity)
    send_xg = jnp.concatenate([to_slots(pick, tokens), to_slots(gate_pick, cotangents)], axis=1)
    send_tan = to_slots(pick, tangents)
    recv_xg = lax.all_to_all(
        send_xg.reshape(expert_count, capacity, 2 * width),
        "expert",
        split_axis=0,
        concat_axis=0,
        tiled=True,
    ).reshape(slots, 2 * width)
    recv_xg, send_tan = lax.optimization_barrier((recv_xg, send_tan))
    tangent = lax.all_to_all(
        send_tan.reshape(expert_count, capacity, width),
        "expert",
        split_axis=0,
        concat_axis=0,
        tiled=True,
    ).reshape(slots, width)
    primal = recv_xg[:, :width]
    scaled_cot = recv_xg[:, width:]
    up_proj = w_up[0]
    down_proj = w_down[0]
    dir_up = v_up[0]
    pre_act = jnp.dot(primal, up_proj, preferred_element_type=jnp.float32)
    sigmoid_z = jax.nn.sigmoid(pre_act)
    first_der = sigmoid_z * (1.0 + pre_act * (1.0 - sigmoid_z))
    second_der = sigmoid_z * (1.0 - sigmoid_z) * (2.0 + pre_act * (1.0 - 2.0 * sigmoid_z))
    back_hid = jnp.dot(scaled_cot, down_proj.T, preferred_element_type=jnp.float32)
    back_pre = (back_hid * first_der).astype(jnp.bfloat16)
    pre_mix = jnp.dot(primal, dir_up, preferred_element_type=jnp.float32)
    hvp_mix = jnp.dot(back_pre, dir_up.T, preferred_element_type=jnp.float32)
    pre_tan = jnp.dot(tangent, up_proj, preferred_element_type=jnp.float32) + pre_mix
    hidden_tan = (first_der * pre_tan).astype(jnp.bfloat16)
    back_tan = (back_hid * second_der * pre_tan).astype(jnp.bfloat16)
    input_hvp = (jnp.dot(back_tan, up_proj.T, preferred_element_type=jnp.float32) + hvp_mix).astype(
        jnp.bfloat16
    )
    returned = lax.all_to_all(
        input_hvp.reshape(expert_count, capacity, width),
        "expert",
        split_axis=0,
        concat_axis=0,
        tiled=True,
    ).reshape(slots, width)
    hvp_tokens = jnp.dot(pick, returned, preferred_element_type=jnp.float32).astype(jnp.bfloat16)
    first = jnp.dot(tangent.T, back_pre, preferred_element_type=jnp.float32) + jnp.dot(
        primal.T, back_tan, preferred_element_type=jnp.float32
    )
    second = jnp.dot(scaled_cot.T, hidden_tan, preferred_element_type=jnp.float32)
    summed = lax.psum_scatter(
        (jnp.concatenate([first, second], axis=1) * scale).astype(jnp.bfloat16),
        "dp",
        scatter_dimension=0,
        tiled=True,
    )
    hidden_units = up_proj.shape[1]
    hvp_up = summed[:, :hidden_units][None]
    hvp_down = summed[:, hidden_units:].T[None]
    return (hvp_tokens, hvp_up, hvp_down)


def solution(mesh):
    in_specs = (
        P(("dp", "expert"), None),
        P(("dp", "expert"), None),
        P(("dp", "expert"), None),
        P(("dp", "expert"), None),
        P(("dp", "expert"), None),
        P("expert", None, None),
        P("expert", None, None),
        P("expert", None, None),
    )
    out_specs = (P(("dp", "expert"), None), P("expert", "dp", None), P("expert", None, "dp"))
    return jax.shard_map(
        per_device, mesh=mesh, in_specs=in_specs, out_specs=out_specs, check_vma=False
    )
```

```python
import math

import jax
import jax.numpy as jnp
from jax import lax
from jax.sharding import PartitionSpec as P


def slot_matrices(route_ids, gate_rows, expert_count, capacity):
    token_count, route_count = route_ids.shape
    routes_total = token_count * route_count
    slots = expert_count * capacity
    flat_ids = route_ids.reshape(routes_total)
    onehot = (flat_ids[:, None] == jnp.arange(expert_count, dtype=jnp.int32)[None, :]).astype(
        jnp.bfloat16
    )
    order = jnp.arange(routes_total, dtype=jnp.int32)
    earlier = (order[None, :] < order[:, None]).astype(jnp.bfloat16)
    before = jnp.dot(earlier, onehot, preferred_element_type=jnp.float32)
    slot_rank = jnp.sum(before * onehot.astype(jnp.float32), axis=1).astype(jnp.int32)
    target = (flat_ids * capacity + slot_rank).reshape(token_count, route_count)
    slot_ids = jnp.arange(slots, dtype=jnp.int32)
    hit = target[:, :, None] == slot_ids[None, None, :]
    pick = jnp.any(hit, axis=1).astype(jnp.bfloat16)
    gate_pick = jnp.sum(
        jnp.where(hit, gate_rows.astype(jnp.float32)[:, :, None], 0.0), axis=1
    ).astype(jnp.bfloat16)
    return pick, gate_pick


def to_slots(pick, rows):
    return lax.dot_general(
        pick, rows, (((0,), (0,)), ((), ())), preferred_element_type=jnp.float32
    ).astype(jnp.bfloat16)


def reduce_over_dp(part, replicas):
    half = replicas // 2
    me = lax.axis_index("dp")
    core = me % 2
    row = me // 2
    blocks = part.reshape(half, 2, part.shape[0] // replicas, part.shape[1])
    keep = lax.dynamic_index_in_dim(blocks, core, axis=1, keepdims=False)
    give = lax.dynamic_index_in_dim(blocks, 1 - core, axis=1, keepdims=False)
    got = lax.ppermute(give, "dp", [(i, i ^ 1) for i in range(replicas)])
    partial = keep.astype(jnp.float32) + got.astype(jnp.float32)
    wire = partial.astype(jnp.bfloat16)
    total = lax.dynamic_index_in_dim(partial, row, axis=0, keepdims=False)
    for step in range(1, half):
        send = lax.dynamic_index_in_dim(wire, (row + step) % half, axis=0, keepdims=False)
        pairs = [(i, (i + 2 * step) % replicas) for i in range(replicas)]
        total = total + lax.ppermute(send, "dp", pairs).astype(jnp.float32)
    return total.astype(jnp.bfloat16)


def per_device(tokens, tangents, cotangents, routes, gates, w_up, w_down, v_up):
    token_count, width = tokens.shape
    route_count = routes.shape[1]
    expert_count = lax.axis_size("expert")
    replicas = lax.axis_size("dp")
    capacity = max(2, token_count * route_count * 2 // expert_count)
    scale = 1.0 / math.sqrt(token_count * route_count * replicas)
    slots = expert_count * capacity
    pick, gate_pick = slot_matrices(routes, gates, expert_count, capacity)
    send_xg = jnp.concatenate([to_slots(pick, tokens), to_slots(gate_pick, cotangents)], axis=1)
    send_tan = to_slots(pick, tangents)
    recv_xg = lax.all_to_all(
        send_xg.reshape(expert_count, capacity, 2 * width),
        "expert",
        split_axis=0,
        concat_axis=0,
        tiled=True,
    ).reshape(slots, 2 * width)
    recv_xg, send_tan = lax.optimization_barrier((recv_xg, send_tan))
    tangent = lax.all_to_all(
        send_tan.reshape(expert_count, capacity, width),
        "expert",
        split_axis=0,
        concat_axis=0,
        tiled=True,
    ).reshape(slots, width)
    primal = recv_xg[:, :width]
    scaled_cot = recv_xg[:, width:]
    up_proj = w_up[0]
    down_proj = w_down[0]
    dir_up = v_up[0]
    pre_act = jnp.dot(primal, up_proj, preferred_element_type=jnp.float32)
    sigmoid_z = jax.nn.sigmoid(pre_act)
    first_der = sigmoid_z * (1.0 + pre_act * (1.0 - sigmoid_z))
    second_der = sigmoid_z * (1.0 - sigmoid_z) * (2.0 + pre_act * (1.0 - 2.0 * sigmoid_z))
    back_hid = jnp.dot(scaled_cot, down_proj.T, preferred_element_type=jnp.float32)
    back_pre = (back_hid * first_der).astype(jnp.bfloat16)
    pre_mix = jnp.dot(primal, dir_up, preferred_element_type=jnp.float32)
    hvp_mix = jnp.dot(back_pre, dir_up.T, preferred_element_type=jnp.float32)
    pre_tan = jnp.dot(tangent, up_proj, preferred_element_type=jnp.float32) + pre_mix
    hidden_tan = (first_der * pre_tan).astype(jnp.bfloat16)
    back_tan = (back_hid * second_der * pre_tan).astype(jnp.bfloat16)
    input_hvp = (jnp.dot(back_tan, up_proj.T, preferred_element_type=jnp.float32) + hvp_mix).astype(
        jnp.bfloat16
    )
    returned = lax.all_to_all(
        input_hvp.reshape(expert_count, capacity, width),
        "expert",
        split_axis=0,
        concat_axis=0,
        tiled=True,
    ).reshape(slots, width)
    second = jnp.dot(scaled_cot.T, hidden_tan, preferred_element_type=jnp.float32)
    down_sum = reduce_over_dp((second * scale).astype(jnp.bfloat16), replicas)
    hvp_tokens = jnp.dot(pick, returned, preferred_element_type=jnp.float32).astype(jnp.bfloat16)
    first = jnp.dot(tangent.T, back_pre, preferred_element_type=jnp.float32) + jnp.dot(
        primal.T, back_tan, preferred_element_type=jnp.float32
    )
    up_sum = reduce_over_dp((first * scale).astype(jnp.bfloat16), replicas)
    hvp_up = up_sum[None]
    hvp_down = down_sum.T[None]
    return (hvp_tokens, hvp_up, hvp_down)


def solution(mesh):
    in_specs = (
        P(("dp", "expert"), None),
        P(("dp", "expert"), None),
        P(("dp", "expert"), None),
        P(("dp", "expert"), None),
        P(("dp", "expert"), None),
        P("expert", None, None),
        P("expert", None, None),
        P("expert", None, None),
    )
    out_specs = (P(("dp", "expert"), None), P("expert", "dp", None), P("expert", None, "dp"))
    return jax.shard_map(
        per_device, mesh=mesh, in_specs=in_specs, out_specs=out_specs, check_vma=False
    )
```

```python
import math

import jax
import jax.numpy as jnp
from jax import lax
from jax.sharding import PartitionSpec as P


def slot_matrices(route_ids, gate_rows, expert_count, capacity):
    token_count, route_count = route_ids.shape
    routes_total = token_count * route_count
    slots = expert_count * capacity
    flat_ids = route_ids.reshape(routes_total)
    onehot = (flat_ids[:, None] == jnp.arange(expert_count, dtype=jnp.int32)[None, :]).astype(
        jnp.bfloat16
    )
    order = jnp.arange(routes_total, dtype=jnp.int32)
    earlier = (order[None, :] < order[:, None]).astype(jnp.bfloat16)
    before = jnp.dot(earlier, onehot, preferred_element_type=jnp.float32)
    slot_rank = jnp.sum(before * onehot.astype(jnp.float32), axis=1).astype(jnp.int32)
    target = (flat_ids * capacity + slot_rank).reshape(token_count, route_count)
    slot_ids = jnp.arange(slots, dtype=jnp.int32)
    hit = target[:, :, None] == slot_ids[None, None, :]
    pick = jnp.any(hit, axis=1).astype(jnp.bfloat16)
    gate_pick = jnp.sum(
        jnp.where(hit, gate_rows.astype(jnp.float32)[:, :, None], 0.0), axis=1
    ).astype(jnp.bfloat16)
    return pick, gate_pick


def to_slots(pick, rows):
    return lax.dot_general(
        pick, rows, (((0,), (0,)), ((), ())), preferred_element_type=jnp.float32
    ).astype(jnp.bfloat16)


def reduce_over_dp(parts, replicas):
    half = replicas // 2
    me = lax.axis_index("dp")
    core = me % 2
    row = me // 2
    rows, cols = parts[0].shape
    blocks = [p.reshape(half, 2, rows // replicas, cols) for p in parts]
    swaps = [(i, i ^ 1) for i in range(replicas)]
    partial = jnp.stack(
        [
            lax.dynamic_index_in_dim(b, core, axis=1, keepdims=False).astype(jnp.float32)
            + lax.ppermute(
                lax.dynamic_index_in_dim(b, 1 - core, axis=1, keepdims=False), "dp", swaps
            ).astype(jnp.float32)
            for b in blocks
        ],
        1,
    )
    rolled = lax.dynamic_slice_in_dim(jnp.concatenate([partial, partial], 0), row, half, 0)
    wire = rolled.astype(jnp.bfloat16)
    total = rolled[0]
    for step in range(1, half):
        pairs = [(i, (i + 2 * step) % replicas) for i in range(replicas)]
        total = total + lax.ppermute(wire[step], "dp", pairs).astype(jnp.float32)
    return total.astype(jnp.bfloat16)


def per_device(tokens, tangents, cotangents, routes, gates, w_up, w_down, v_up):
    token_count, width = tokens.shape
    route_count = routes.shape[1]
    expert_count = lax.axis_size("expert")
    replicas = lax.axis_size("dp")
    capacity = max(2, token_count * route_count * 2 // expert_count)
    scale = 1.0 / math.sqrt(token_count * route_count * replicas)
    slots = expert_count * capacity
    pick, gate_pick = slot_matrices(routes, gates, expert_count, capacity)
    send_xg = jnp.concatenate([to_slots(pick, tokens), to_slots(gate_pick, cotangents)], axis=1)
    send_tan = to_slots(pick, tangents)
    recv_xg = lax.all_to_all(
        send_xg.reshape(expert_count, capacity, 2 * width),
        "expert",
        split_axis=0,
        concat_axis=0,
        tiled=True,
    ).reshape(slots, 2 * width)
    recv_xg, send_tan = lax.optimization_barrier((recv_xg, send_tan))
    tangent = lax.all_to_all(
        send_tan.reshape(expert_count, capacity, width),
        "expert",
        split_axis=0,
        concat_axis=0,
        tiled=True,
    ).reshape(slots, width)
    primal = recv_xg[:, :width]
    scaled_cot = recv_xg[:, width:]
    up_proj = w_up[0]
    down_proj = w_down[0]
    dir_up = v_up[0]
    pre_act = jnp.dot(primal, up_proj, preferred_element_type=jnp.float32)
    sigmoid_z = jax.nn.sigmoid(pre_act)
    first_der = sigmoid_z * (1.0 + pre_act * (1.0 - sigmoid_z))
    second_der = sigmoid_z * (1.0 - sigmoid_z) * (2.0 + pre_act * (1.0 - 2.0 * sigmoid_z))
    back_hid = jnp.dot(scaled_cot, down_proj.T, preferred_element_type=jnp.float32)
    back_pre = (back_hid * first_der).astype(jnp.bfloat16)
    pre_mix = jnp.dot(primal, dir_up, preferred_element_type=jnp.float32)
    hvp_mix = jnp.dot(back_pre, dir_up.T, preferred_element_type=jnp.float32)
    pre_tan = jnp.dot(tangent, up_proj, preferred_element_type=jnp.float32) + pre_mix
    hidden_tan = (first_der * pre_tan).astype(jnp.bfloat16)
    back_tan = (back_hid * second_der * pre_tan).astype(jnp.bfloat16)
    input_hvp = (jnp.dot(back_tan, up_proj.T, preferred_element_type=jnp.float32) + hvp_mix).astype(
        jnp.bfloat16
    )
    returned = lax.all_to_all(
        input_hvp.reshape(expert_count, capacity, width),
        "expert",
        split_axis=0,
        concat_axis=0,
        tiled=True,
    ).reshape(slots, width)
    hvp_tokens = jnp.dot(pick, returned, preferred_element_type=jnp.float32).astype(jnp.bfloat16)
    second = jnp.dot(scaled_cot.T, hidden_tan, preferred_element_type=jnp.float32)
    first = jnp.dot(tangent.T, back_pre, preferred_element_type=jnp.float32) + jnp.dot(
        primal.T, back_tan, preferred_element_type=jnp.float32
    )
    summed = reduce_over_dp(
        ((first * scale).astype(jnp.bfloat16), (second * scale).astype(jnp.bfloat16)), replicas
    )
    hvp_up = summed[0][None]
    hvp_down = summed[1].T[None]
    return (hvp_tokens, hvp_up, hvp_down)


def solution(mesh):
    in_specs = (
        P(("dp", "expert"), None),
        P(("dp", "expert"), None),
        P(("dp", "expert"), None),
        P(("dp", "expert"), None),
        P(("dp", "expert"), None),
        P("expert", None, None),
        P("expert", None, None),
        P("expert", None, None),
    )
    out_specs = (P(("dp", "expert"), None), P("expert", "dp", None), P("expert", None, "dp"))
    return jax.shard_map(
        per_device, mesh=mesh, in_specs=in_specs, out_specs=out_specs, check_vma=False
    )
```

```python
import math

import jax
import jax.numpy as jnp
from jax import lax
from jax.sharding import PartitionSpec as P


def slot_matrices(route_ids, gate_rows, expert_count, capacity):
    token_count, route_count = route_ids.shape
    routes_total = token_count * route_count
    slots = expert_count * capacity
    flat_ids = route_ids.reshape(routes_total)
    onehot = (flat_ids[:, None] == jnp.arange(expert_count, dtype=jnp.int32)[None, :]).astype(
        jnp.bfloat16
    )
    order = jnp.arange(routes_total, dtype=jnp.int32)
    earlier = (order[None, :] < order[:, None]).astype(jnp.bfloat16)
    before = jnp.dot(earlier, onehot, preferred_element_type=jnp.float32)
    slot_rank = jnp.sum(before * onehot.astype(jnp.float32), axis=1).astype(jnp.int32)
    target = (flat_ids * capacity + slot_rank).reshape(token_count, route_count)
    slot_ids = jnp.arange(slots, dtype=jnp.int32)
    hit = target[:, :, None] == slot_ids[None, None, :]
    pick = jnp.any(hit, axis=1).astype(jnp.bfloat16)
    gate_pick = jnp.sum(
        jnp.where(hit, gate_rows.astype(jnp.float32)[:, :, None], 0.0), axis=1
    ).astype(jnp.bfloat16)
    return pick, gate_pick


def to_slots(pick, rows):
    return lax.dot_general(
        pick, rows, (((0,), (0,)), ((), ())), preferred_element_type=jnp.float32
    ).astype(jnp.bfloat16)


def reduce_over_dp(part, replicas):
    half = replicas // 2
    me = lax.axis_index("dp")
    core = me % 2
    row = me // 2
    blocks = part.reshape(half, 2, part.shape[0] // replicas, part.shape[1])
    keep = lax.dynamic_index_in_dim(blocks, core, axis=1, keepdims=False)
    give = lax.dynamic_index_in_dim(blocks, 1 - core, axis=1, keepdims=False)
    got = lax.ppermute(give, "dp", [(i, i ^ 1) for i in range(replicas)])
    partial = keep.astype(jnp.float32) + got.astype(jnp.float32)
    wire = partial.astype(jnp.bfloat16)
    wire = lax.dynamic_slice_in_dim(jnp.concatenate([wire, wire], 0), row, half, 0)
    total = lax.dynamic_index_in_dim(partial, row, axis=0, keepdims=False)
    for step in range(1, half):
        pairs = [(i, (i + 2 * step) % replicas) for i in range(replicas)]
        total = total + lax.ppermute(wire[step], "dp", pairs).astype(jnp.float32)
    return total.astype(jnp.bfloat16)


def per_device(tokens, tangents, cotangents, routes, gates, w_up, w_down, v_up):
    token_count, width = tokens.shape
    route_count = routes.shape[1]
    expert_count = lax.axis_size("expert")
    replicas = lax.axis_size("dp")
    capacity = max(2, token_count * route_count * 2 // expert_count)
    scale = 1.0 / math.sqrt(token_count * route_count * replicas)
    slots = expert_count * capacity
    pick, gate_pick = slot_matrices(routes, gates, expert_count, capacity)
    send_xg = jnp.concatenate([to_slots(pick, tokens), to_slots(gate_pick, cotangents)], axis=1)
    send_tan = to_slots(pick, tangents)
    recv_xg = lax.all_to_all(
        send_xg.reshape(expert_count, capacity, 2 * width),
        "expert",
        split_axis=0,
        concat_axis=0,
        tiled=True,
    ).reshape(slots, 2 * width)
    recv_xg, send_tan = lax.optimization_barrier((recv_xg, send_tan))
    tangent = lax.all_to_all(
        send_tan.reshape(expert_count, capacity, width),
        "expert",
        split_axis=0,
        concat_axis=0,
        tiled=True,
    ).reshape(slots, width)
    primal = recv_xg[:, :width]
    scaled_cot = recv_xg[:, width:]
    up_proj = w_up[0]
    down_proj = w_down[0]
    dir_up = v_up[0]
    pre_act = jnp.dot(primal, up_proj, preferred_element_type=jnp.float32)
    sigmoid_z = jax.nn.sigmoid(pre_act)
    first_der = sigmoid_z * (1.0 + pre_act * (1.0 - sigmoid_z))
    second_der = sigmoid_z * (1.0 - sigmoid_z) * (2.0 + pre_act * (1.0 - 2.0 * sigmoid_z))
    back_hid = jnp.dot(scaled_cot, down_proj.T, preferred_element_type=jnp.float32)
    back_pre = (back_hid * first_der).astype(jnp.bfloat16)
    pre_mix = jnp.dot(primal, dir_up, preferred_element_type=jnp.float32)
    hvp_mix = jnp.dot(back_pre, dir_up.T, preferred_element_type=jnp.float32)
    pre_tan = jnp.dot(tangent, up_proj, preferred_element_type=jnp.float32) + pre_mix
    hidden_tan = (first_der * pre_tan).astype(jnp.bfloat16)
    back_tan = (back_hid * second_der * pre_tan).astype(jnp.bfloat16)
    input_hvp = (jnp.dot(back_tan, up_proj.T, preferred_element_type=jnp.float32) + hvp_mix).astype(
        jnp.bfloat16
    )
    returned = lax.all_to_all(
        input_hvp.reshape(expert_count, capacity, width),
        "expert",
        split_axis=0,
        concat_axis=0,
        tiled=True,
    ).reshape(slots, width)
    second = jnp.dot(scaled_cot.T, hidden_tan, preferred_element_type=jnp.float32)
    down_sum = reduce_over_dp((second * scale).astype(jnp.bfloat16), replicas)
    hvp_tokens = jnp.dot(pick, returned, preferred_element_type=jnp.float32).astype(jnp.bfloat16)
    first = jnp.dot(tangent.T, back_pre, preferred_element_type=jnp.float32) + jnp.dot(
        primal.T, back_tan, preferred_element_type=jnp.float32
    )
    up_sum = reduce_over_dp((first * scale).astype(jnp.bfloat16), replicas)
    hvp_up = up_sum[None]
    hvp_down = down_sum.T[None]
    return (hvp_tokens, hvp_up, hvp_down)


def solution(mesh):
    in_specs = (
        P(("dp", "expert"), None),
        P(("dp", "expert"), None),
        P(("dp", "expert"), None),
        P(("dp", "expert"), None),
        P(("dp", "expert"), None),
        P("expert", None, None),
        P("expert", None, None),
        P("expert", None, None),
    )
    out_specs = (P(("dp", "expert"), None), P("expert", "dp", None), P("expert", None, "dp"))
    return jax.shard_map(
        per_device, mesh=mesh, in_specs=in_specs, out_specs=out_specs, check_vma=False
    )
```

```python
import math

import jax
import jax.numpy as jnp
from jax import lax
from jax.sharding import PartitionSpec as P


def slot_matrices(route_ids, gate_rows, expert_count, capacity):
    token_count, route_count = route_ids.shape
    routes_total = token_count * route_count
    slots = expert_count * capacity
    flat_ids = route_ids.reshape(routes_total)
    onehot = (flat_ids[:, None] == jnp.arange(expert_count, dtype=jnp.int32)[None, :]).astype(
        jnp.bfloat16
    )
    order = jnp.arange(routes_total, dtype=jnp.int32)
    earlier = (order[None, :] < order[:, None]).astype(jnp.bfloat16)
    before = jnp.dot(earlier, onehot, preferred_element_type=jnp.float32)
    slot_rank = jnp.sum(before * onehot.astype(jnp.float32), axis=1).astype(jnp.int32)
    target = (flat_ids * capacity + slot_rank).reshape(token_count, route_count)
    slot_ids = jnp.arange(slots, dtype=jnp.int32)
    hit = target[:, :, None] == slot_ids[None, None, :]
    pick = jnp.any(hit, axis=1).astype(jnp.bfloat16)
    gate_pick = jnp.sum(
        jnp.where(hit, gate_rows.astype(jnp.float32)[:, :, None], 0.0), axis=1
    ).astype(jnp.bfloat16)
    return pick, gate_pick


def to_slots(pick, rows):
    return lax.dot_general(
        pick, rows, (((0,), (0,)), ((), ())), preferred_element_type=jnp.float32
    ).astype(jnp.bfloat16)


def reduce_over_dp(part, replicas):
    half = replicas // 2
    me = lax.axis_index("dp")
    core = me % 2
    row = me // 2
    blocks = part.reshape(half, 2, part.shape[0] // replicas, part.shape[1])
    keep = lax.dynamic_index_in_dim(blocks, core, axis=1, keepdims=False)
    give = lax.dynamic_index_in_dim(blocks, 1 - core, axis=1, keepdims=False)
    got = lax.ppermute(give, "dp", [(i, i ^ 1) for i in range(replicas)])
    partial = keep.astype(jnp.float32) + got.astype(jnp.float32)
    wire = partial.astype(jnp.bfloat16)
    wire = lax.dynamic_slice_in_dim(jnp.concatenate([wire, wire], 0), row, half, 0)
    total = lax.dynamic_index_in_dim(partial, row, axis=0, keepdims=False)
    for step in range(1, half):
        pairs = [(i, (i + 2 * step) % replicas) for i in range(replicas)]
        total = total + lax.ppermute(wire[step], "dp", pairs).astype(jnp.float32)
    return total.astype(jnp.bfloat16)


def per_device(tokens, tangents, cotangents, routes, gates, w_up, w_down, v_up):
    token_count, width = tokens.shape
    route_count = routes.shape[1]
    expert_count = lax.axis_size("expert")
    replicas = lax.axis_size("dp")
    capacity = max(2, token_count * route_count * 2 // expert_count)
    scale = 1.0 / math.sqrt(token_count * route_count * replicas)
    slots = expert_count * capacity
    pick, gate_pick = slot_matrices(routes, gates, expert_count, capacity)
    send_xg = jnp.concatenate([to_slots(pick, tokens), to_slots(gate_pick, cotangents)], axis=1)
    send_tan = to_slots(pick, tangents)
    recv_xg = lax.all_to_all(
        send_xg.reshape(expert_count, capacity, 2 * width),
        "expert",
        split_axis=0,
        concat_axis=0,
        tiled=True,
    ).reshape(slots, 2 * width)
    recv_xg, send_tan = lax.optimization_barrier((recv_xg, send_tan))
    tangent = lax.all_to_all(
        send_tan.reshape(expert_count, capacity, width),
        "expert",
        split_axis=0,
        concat_axis=0,
        tiled=True,
    ).reshape(slots, width)
    primal = recv_xg[:, :width]
    scaled_cot = recv_xg[:, width:]
    up_proj = w_up[0]
    down_proj = w_down[0]
    dir_up = v_up[0]
    pre_act = jnp.dot(primal, up_proj, preferred_element_type=jnp.float32)
    sigmoid_z = jax.nn.sigmoid(pre_act)
    first_der = sigmoid_z * (1.0 + pre_act * (1.0 - sigmoid_z))
    second_der = sigmoid_z * (1.0 - sigmoid_z) * (2.0 + pre_act * (1.0 - 2.0 * sigmoid_z))
    back_hid = jnp.dot(scaled_cot, down_proj.T, preferred_element_type=jnp.float32)
    back_pre = (back_hid * first_der).astype(jnp.bfloat16)
    pre_mix = jnp.dot(primal, dir_up, preferred_element_type=jnp.float32)
    hvp_mix = jnp.dot(back_pre, dir_up.T, preferred_element_type=jnp.float32)
    pre_tan = jnp.dot(tangent, up_proj, preferred_element_type=jnp.float32) + pre_mix
    hidden_tan = (first_der * pre_tan).astype(jnp.bfloat16)
    back_tan = (back_hid * second_der * pre_tan).astype(jnp.bfloat16)
    input_hvp = (jnp.dot(back_tan, up_proj.T, preferred_element_type=jnp.float32) + hvp_mix).astype(
        jnp.bfloat16
    )
    input_hvp, back_pre, back_tan, hidden_tan = lax.optimization_barrier(
        (input_hvp, back_pre, back_tan, hidden_tan)
    )
    returned = lax.all_to_all(
        input_hvp.reshape(expert_count, capacity, width),
        "expert",
        split_axis=0,
        concat_axis=0,
        tiled=True,
    ).reshape(slots, width)
    second = jnp.dot(scaled_cot.T, hidden_tan, preferred_element_type=jnp.float32)
    down_sum = reduce_over_dp((second * scale).astype(jnp.bfloat16), replicas)
    hvp_tokens = jnp.dot(pick, returned, preferred_element_type=jnp.float32).astype(jnp.bfloat16)
    first = jnp.dot(tangent.T, back_pre, preferred_element_type=jnp.float32) + jnp.dot(
        primal.T, back_tan, preferred_element_type=jnp.float32
    )
    up_sum = reduce_over_dp((first * scale).astype(jnp.bfloat16), replicas)
    hvp_up = up_sum[None]
    hvp_down = down_sum.T[None]
    return (hvp_tokens, hvp_up, hvp_down)


def solution(mesh):
    in_specs = (
        P(("dp", "expert"), None),
        P(("dp", "expert"), None),
        P(("dp", "expert"), None),
        P(("dp", "expert"), None),
        P(("dp", "expert"), None),
        P("expert", None, None),
        P("expert", None, None),
        P("expert", None, None),
    )
    out_specs = (P(("dp", "expert"), None), P("expert", "dp", None), P("expert", None, "dp"))
    return jax.shard_map(
        per_device, mesh=mesh, in_specs=in_specs, out_specs=out_specs, check_vma=False
    )
```

```python
import math

import jax
import jax.numpy as jnp
from jax import lax
from jax.sharding import PartitionSpec as P


def slot_matrices(route_ids, gate_rows, expert_count, capacity):
    token_count, route_count = route_ids.shape
    routes_total = token_count * route_count
    slots = expert_count * capacity
    flat_ids = route_ids.reshape(routes_total)
    onehot = (flat_ids[:, None] == jnp.arange(expert_count, dtype=jnp.int32)[None, :]).astype(
        jnp.bfloat16
    )
    order = jnp.arange(routes_total, dtype=jnp.int32)
    earlier = (order[None, :] < order[:, None]).astype(jnp.bfloat16)
    before = jnp.dot(earlier, onehot, preferred_element_type=jnp.float32)
    slot_rank = jnp.sum(before * onehot.astype(jnp.float32), axis=1).astype(jnp.int32)
    target = (flat_ids * capacity + slot_rank).reshape(token_count, route_count)
    slot_ids = jnp.arange(slots, dtype=jnp.int32)
    hit = target[:, :, None] == slot_ids[None, None, :]
    pick = jnp.any(hit, axis=1).astype(jnp.bfloat16)
    gate_slot = jnp.sum(jnp.where(hit, gate_rows.astype(jnp.float32)[:, :, None], 0.0), axis=(0, 1))
    return pick, gate_slot


def to_slots(pick, rows):
    return lax.dot_general(
        pick, rows, (((0,), (0,)), ((), ())), preferred_element_type=jnp.float32
    ).astype(jnp.bfloat16)


def reduce_over_dp(part, replicas):
    half = replicas // 2
    me = lax.axis_index("dp")
    core = me % 2
    row = me // 2
    blocks = part.reshape(half, 2, part.shape[0] // replicas, part.shape[1])
    keep = lax.dynamic_index_in_dim(blocks, core, axis=1, keepdims=False)
    give = lax.dynamic_index_in_dim(blocks, 1 - core, axis=1, keepdims=False)
    got = lax.ppermute(give, "dp", [(i, i ^ 1) for i in range(replicas)])
    partial = keep.astype(jnp.float32) + got.astype(jnp.float32)
    wire = partial.astype(jnp.bfloat16)
    wire = lax.dynamic_slice_in_dim(jnp.concatenate([wire, wire], 0), row, half, 0)
    total = lax.dynamic_index_in_dim(partial, row, axis=0, keepdims=False)
    for step in range(1, half):
        pairs = [(i, (i + 2 * step) % replicas) for i in range(replicas)]
        total = total + lax.ppermute(wire[step], "dp", pairs).astype(jnp.float32)
    return total.astype(jnp.bfloat16)


def per_device(tokens, tangents, cotangents, routes, gates, w_up, w_down, v_up):
    token_count, width = tokens.shape
    route_count = routes.shape[1]
    expert_count = lax.axis_size("expert")
    replicas = lax.axis_size("dp")
    capacity = max(2, token_count * route_count * 2 // expert_count)
    scale = 1.0 / math.sqrt(token_count * route_count * replicas)
    slots = expert_count * capacity
    pick, gate_slot = slot_matrices(routes, gates, expert_count, capacity)
    rows_xg = lax.dot_general(
        pick,
        jnp.concatenate([tokens, cotangents], axis=1),
        (((0,), (0,)), ((), ())),
        preferred_element_type=jnp.float32,
    )
    column = jnp.arange(2 * width, dtype=jnp.int32)[None, :]
    send_xg = (rows_xg * jnp.where(column < width, 1.0, gate_slot[:, None])).astype(jnp.bfloat16)
    send_tan = to_slots(pick, tangents)
    recv_xg = lax.all_to_all(
        send_xg.reshape(expert_count, capacity, 2 * width),
        "expert",
        split_axis=0,
        concat_axis=0,
        tiled=True,
    ).reshape(slots, 2 * width)
    recv_xg, send_tan = lax.optimization_barrier((recv_xg, send_tan))
    tangent = lax.all_to_all(
        send_tan.reshape(expert_count, capacity, width),
        "expert",
        split_axis=0,
        concat_axis=0,
        tiled=True,
    ).reshape(slots, width)
    primal = recv_xg[:, :width]
    scaled_cot = recv_xg[:, width:]
    up_proj = w_up[0]
    down_proj = w_down[0]
    dir_up = v_up[0]
    pre_act = jnp.dot(primal, up_proj, preferred_element_type=jnp.float32)
    sigmoid_z = jax.nn.sigmoid(pre_act)
    first_der = sigmoid_z * (1.0 + pre_act * (1.0 - sigmoid_z))
    second_der = sigmoid_z * (1.0 - sigmoid_z) * (2.0 + pre_act * (1.0 - 2.0 * sigmoid_z))
    back_hid = jnp.dot(scaled_cot, down_proj.T, preferred_element_type=jnp.float32)
    back_pre = (back_hid * first_der).astype(jnp.bfloat16)
    pre_mix = jnp.dot(primal, dir_up, preferred_element_type=jnp.float32)
    hvp_mix = jnp.dot(back_pre, dir_up.T, preferred_element_type=jnp.float32)
    pre_tan = jnp.dot(tangent, up_proj, preferred_element_type=jnp.float32) + pre_mix
    hidden_tan = (first_der * pre_tan).astype(jnp.bfloat16)
    back_tan = (back_hid * second_der * pre_tan).astype(jnp.bfloat16)
    input_hvp = (jnp.dot(back_tan, up_proj.T, preferred_element_type=jnp.float32) + hvp_mix).astype(
        jnp.bfloat16
    )
    input_hvp, back_pre, back_tan, hidden_tan = lax.optimization_barrier(
        (input_hvp, back_pre, back_tan, hidden_tan)
    )
    returned = lax.all_to_all(
        input_hvp.reshape(expert_count, capacity, width),
        "expert",
        split_axis=0,
        concat_axis=0,
        tiled=True,
    ).reshape(slots, width)
    second = jnp.dot(scaled_cot.T, hidden_tan, preferred_element_type=jnp.float32)
    down_sum = reduce_over_dp((second * scale).astype(jnp.bfloat16), replicas)
    hvp_tokens = jnp.dot(pick, returned, preferred_element_type=jnp.float32).astype(jnp.bfloat16)
    first = jnp.dot(tangent.T, back_pre, preferred_element_type=jnp.float32) + jnp.dot(
        primal.T, back_tan, preferred_element_type=jnp.float32
    )
    up_sum = reduce_over_dp((first * scale).astype(jnp.bfloat16), replicas)
    hvp_up = up_sum[None]
    hvp_down = down_sum.T[None]
    return (hvp_tokens, hvp_up, hvp_down)


def solution(mesh):
    in_specs = (
        P(("dp", "expert"), None),
        P(("dp", "expert"), None),
        P(("dp", "expert"), None),
        P(("dp", "expert"), None),
        P(("dp", "expert"), None),
        P("expert", None, None),
        P("expert", None, None),
        P("expert", None, None),
    )
    out_specs = (P(("dp", "expert"), None), P("expert", "dp", None), P("expert", None, "dp"))
    return jax.shard_map(
        per_device, mesh=mesh, in_specs=in_specs, out_specs=out_specs, check_vma=False
    )
```

```python
import math

import jax
import jax.numpy as jnp
from jax import lax
from jax.sharding import PartitionSpec as P


def slot_matrices(route_ids, gate_rows, expert_count, capacity):
    token_count, route_count = route_ids.shape
    routes_total = token_count * route_count
    slots = expert_count * capacity
    flat_ids = route_ids.reshape(routes_total)
    onehot = (flat_ids[:, None] == jnp.arange(expert_count, dtype=jnp.int32)[None, :]).astype(
        jnp.bfloat16
    )
    order = jnp.arange(routes_total, dtype=jnp.int32)
    earlier = (order[None, :] < order[:, None]).astype(jnp.bfloat16)
    before = jnp.dot(earlier, onehot, preferred_element_type=jnp.float32)
    slot_rank = jnp.sum(before * onehot.astype(jnp.float32), axis=1).astype(jnp.int32)
    target = (flat_ids * capacity + slot_rank).reshape(token_count, route_count)
    slot_ids = jnp.arange(slots, dtype=jnp.int32)
    hit = target[:, :, None] == slot_ids[None, None, :]
    pick = jnp.any(hit, axis=1).astype(jnp.bfloat16)
    gate_slot = jnp.sum(jnp.where(hit, gate_rows.astype(jnp.float32)[:, :, None], 0.0), axis=(0, 1))
    return pick, gate_slot


def to_slots(pick, rows):
    return lax.dot_general(
        pick, rows, (((0,), (0,)), ((), ())), preferred_element_type=jnp.float32
    ).astype(jnp.bfloat16)


def reduce_over_dp(part, replicas):
    half = replicas // 2
    me = lax.axis_index("dp")
    core = me % 2
    row = me // 2
    blocks = part.reshape(half, 2, part.shape[0] // replicas, part.shape[1])
    keep = lax.dynamic_index_in_dim(blocks, core, axis=1, keepdims=False)
    give = lax.dynamic_index_in_dim(blocks, 1 - core, axis=1, keepdims=False)
    got = lax.ppermute(give, "dp", [(i, i ^ 1) for i in range(replicas)])
    partial = keep.astype(jnp.float32) + got.astype(jnp.float32)
    wire = partial.astype(jnp.bfloat16)
    wire = lax.dynamic_slice_in_dim(jnp.concatenate([wire, wire], 0), row, half, 0)
    total = lax.dynamic_index_in_dim(partial, row, axis=0, keepdims=False)
    for step in range(1, half):
        pairs = [(i, (i + 2 * step) % replicas) for i in range(replicas)]
        total = total + lax.ppermute(wire[step], "dp", pairs).astype(jnp.float32)
    return total.astype(jnp.bfloat16)


def per_device(tokens, tangents, cotangents, routes, gates, w_up, w_down, v_up):
    token_count, width = tokens.shape
    route_count = routes.shape[1]
    expert_count = lax.axis_size("expert")
    replicas = lax.axis_size("dp")
    capacity = max(2, token_count * route_count * 2 // expert_count)
    scale = 1.0 / math.sqrt(token_count * route_count * replicas)
    slots = expert_count * capacity
    pick, gate_slot = slot_matrices(routes, gates, expert_count, capacity)
    rows_xg = lax.dot_general(
        pick,
        jnp.concatenate([tokens, cotangents], axis=1),
        (((0,), (0,)), ((), ())),
        preferred_element_type=jnp.float32,
    )
    column = jnp.arange(2 * width, dtype=jnp.int32)[None, :]
    send_xg = (rows_xg * jnp.where(column < width, 1.0, gate_slot[:, None])).astype(jnp.bfloat16)
    send_tan = to_slots(pick, tangents)
    recv_xg = lax.all_to_all(
        send_xg.reshape(expert_count, capacity, 2 * width),
        "expert",
        split_axis=0,
        concat_axis=0,
        tiled=True,
    ).reshape(slots, 2 * width)
    recv_xg, send_tan = lax.optimization_barrier((recv_xg, send_tan))
    tangent = lax.all_to_all(
        send_tan.reshape(expert_count, capacity, width),
        "expert",
        split_axis=0,
        concat_axis=0,
        tiled=True,
    ).reshape(slots, width)
    primal = recv_xg[:, :width]
    scaled_cot = recv_xg[:, width:]
    up_proj = w_up[0]
    down_proj = w_down[0]
    dir_up = v_up[0]
    pre_act = jnp.dot(primal, up_proj, preferred_element_type=jnp.float32)
    sigmoid_z = jax.nn.sigmoid(pre_act)
    first_der = sigmoid_z * (1.0 + pre_act * (1.0 - sigmoid_z))
    second_der = sigmoid_z * (1.0 - sigmoid_z) * (2.0 + pre_act * (1.0 - 2.0 * sigmoid_z))
    back_hid = jnp.dot(scaled_cot, down_proj.T, preferred_element_type=jnp.float32)
    back_pre = (back_hid * first_der).astype(jnp.bfloat16)
    pre_mix = jnp.dot(primal, dir_up, preferred_element_type=jnp.float32)
    hvp_mix = jnp.dot(back_pre, dir_up.T, preferred_element_type=jnp.float32)
    pre_tan = jnp.dot(tangent, up_proj, preferred_element_type=jnp.float32) + pre_mix
    hidden_tan = (first_der * pre_tan).astype(jnp.bfloat16)
    back_tan = (back_hid * second_der * pre_tan).astype(jnp.bfloat16)
    input_hvp = (jnp.dot(back_tan, up_proj.T, preferred_element_type=jnp.float32) + hvp_mix).astype(
        jnp.bfloat16
    )
    second = jnp.dot(scaled_cot.T, hidden_tan, preferred_element_type=jnp.float32)
    down_part = (second * scale).astype(jnp.bfloat16)
    input_hvp, back_pre, back_tan, down_part = lax.optimization_barrier(
        (input_hvp, back_pre, back_tan, down_part)
    )
    returned = lax.all_to_all(
        input_hvp.reshape(expert_count, capacity, width),
        "expert",
        split_axis=0,
        concat_axis=0,
        tiled=True,
    ).reshape(slots, width)
    down_sum = reduce_over_dp(down_part, replicas)
    hvp_tokens = jnp.dot(pick, returned, preferred_element_type=jnp.float32).astype(jnp.bfloat16)
    first = jnp.dot(tangent.T, back_pre, preferred_element_type=jnp.float32) + jnp.dot(
        primal.T, back_tan, preferred_element_type=jnp.float32
    )
    up_sum = reduce_over_dp((first * scale).astype(jnp.bfloat16), replicas)
    hvp_up = up_sum[None]
    hvp_down = down_sum.T[None]
    return (hvp_tokens, hvp_up, hvp_down)


def solution(mesh):
    in_specs = (
        P(("dp", "expert"), None),
        P(("dp", "expert"), None),
        P(("dp", "expert"), None),
        P(("dp", "expert"), None),
        P(("dp", "expert"), None),
        P("expert", None, None),
        P("expert", None, None),
        P("expert", None, None),
    )
    out_specs = (P(("dp", "expert"), None), P("expert", "dp", None), P("expert", None, "dp"))
    return jax.shard_map(
        per_device, mesh=mesh, in_specs=in_specs, out_specs=out_specs, check_vma=False
    )
```

```python
import math

import jax
import jax.numpy as jnp
from jax import lax
from jax.sharding import PartitionSpec as P


def slot_matrices(route_ids, gate_rows, expert_count, capacity):
    token_count, route_count = route_ids.shape
    routes_total = token_count * route_count
    slots = expert_count * capacity
    flat_ids = route_ids.reshape(routes_total)
    onehot = (flat_ids[:, None] == jnp.arange(expert_count, dtype=jnp.int32)[None, :]).astype(
        jnp.bfloat16
    )
    order = jnp.arange(routes_total, dtype=jnp.int32)
    earlier = (order[None, :] < order[:, None]).astype(jnp.bfloat16)
    before = jnp.dot(earlier, onehot, preferred_element_type=jnp.float32)
    slot_rank = jnp.sum(before * onehot.astype(jnp.float32), axis=1).astype(jnp.int32)
    target = (flat_ids * capacity + slot_rank).reshape(token_count, route_count)
    slot_ids = jnp.arange(slots, dtype=jnp.int32)
    hit = target[:, :, None] == slot_ids[None, None, :]
    pick = jnp.any(hit, axis=1).astype(jnp.bfloat16)
    gate_slot = jnp.sum(jnp.where(hit, gate_rows.astype(jnp.float32)[:, :, None], 0.0), axis=(0, 1))
    return pick, gate_slot


def to_slots(pick, rows):
    return lax.dot_general(
        pick, rows, (((0,), (0,)), ((), ())), preferred_element_type=jnp.float32
    ).astype(jnp.bfloat16)


def reduce_over_dp(part, replicas, anchor=None):
    half = replicas // 2
    me = lax.axis_index("dp")
    core = me % 2
    row = me // 2
    blocks = part.reshape(half, 2, part.shape[0] // replicas, part.shape[1])
    keep = lax.dynamic_index_in_dim(blocks, core, axis=1, keepdims=False)
    give = lax.dynamic_index_in_dim(blocks, 1 - core, axis=1, keepdims=False)
    got = lax.ppermute(give, "dp", [(i, i ^ 1) for i in range(replicas)])
    partial = keep.astype(jnp.float32) + got.astype(jnp.float32)
    wire = partial.astype(jnp.bfloat16)
    wire = lax.dynamic_slice_in_dim(jnp.concatenate([wire, wire], 0), row, half, 0)
    received = []
    for step in range(1, half):
        pairs = [(i, (i + 2 * step) % replicas) for i in range(replicas)]
        received.append(lax.ppermute(wire[step], "dp", pairs))
    if anchor is not None:
        anchor, received = lax.optimization_barrier((anchor, received))
    total = lax.dynamic_index_in_dim(partial, row, axis=0, keepdims=False)
    for piece in received:
        total = total + piece.astype(jnp.float32)
    return total.astype(jnp.bfloat16), anchor


def per_device(tokens, tangents, cotangents, routes, gates, w_up, w_down, v_up):
    token_count, width = tokens.shape
    route_count = routes.shape[1]
    expert_count = lax.axis_size("expert")
    replicas = lax.axis_size("dp")
    capacity = max(2, token_count * route_count * 2 // expert_count)
    scale = 1.0 / math.sqrt(token_count * route_count * replicas)
    slots = expert_count * capacity
    pick, gate_slot = slot_matrices(routes, gates, expert_count, capacity)
    rows_xg = lax.dot_general(
        pick,
        jnp.concatenate([tokens, cotangents], axis=1),
        (((0,), (0,)), ((), ())),
        preferred_element_type=jnp.float32,
    )
    column = jnp.arange(2 * width, dtype=jnp.int32)[None, :]
    send_xg = (rows_xg * jnp.where(column < width, 1.0, gate_slot[:, None])).astype(jnp.bfloat16)
    send_tan = to_slots(pick, tangents)
    recv_xg = lax.all_to_all(
        send_xg.reshape(expert_count, capacity, 2 * width),
        "expert",
        split_axis=0,
        concat_axis=0,
        tiled=True,
    ).reshape(slots, 2 * width)
    recv_xg, send_tan = lax.optimization_barrier((recv_xg, send_tan))
    tangent = lax.all_to_all(
        send_tan.reshape(expert_count, capacity, width),
        "expert",
        split_axis=0,
        concat_axis=0,
        tiled=True,
    ).reshape(slots, width)
    primal = recv_xg[:, :width]
    scaled_cot = recv_xg[:, width:]
    up_proj = w_up[0]
    down_proj = w_down[0]
    dir_up = v_up[0]
    pre_act = jnp.dot(primal, up_proj, preferred_element_type=jnp.float32)
    sigmoid_z = jax.nn.sigmoid(pre_act)
    first_der = sigmoid_z * (1.0 + pre_act * (1.0 - sigmoid_z))
    second_der = sigmoid_z * (1.0 - sigmoid_z) * (2.0 + pre_act * (1.0 - 2.0 * sigmoid_z))
    back_hid = jnp.dot(scaled_cot, down_proj.T, preferred_element_type=jnp.float32)
    back_pre = (back_hid * first_der).astype(jnp.bfloat16)
    pre_mix = jnp.dot(primal, dir_up, preferred_element_type=jnp.float32)
    hvp_mix = jnp.dot(back_pre, dir_up.T, preferred_element_type=jnp.float32)
    pre_tan = jnp.dot(tangent, up_proj, preferred_element_type=jnp.float32) + pre_mix
    hidden_tan = (first_der * pre_tan).astype(jnp.bfloat16)
    back_tan = (back_hid * second_der * pre_tan).astype(jnp.bfloat16)
    input_hvp = (jnp.dot(back_tan, up_proj.T, preferred_element_type=jnp.float32) + hvp_mix).astype(
        jnp.bfloat16
    )
    input_hvp, back_pre, back_tan, hidden_tan = lax.optimization_barrier(
        (input_hvp, back_pre, back_tan, hidden_tan)
    )
    returned = lax.all_to_all(
        input_hvp.reshape(expert_count, capacity, width),
        "expert",
        split_axis=0,
        concat_axis=0,
        tiled=True,
    ).reshape(slots, width)
    second = jnp.dot(scaled_cot.T, hidden_tan, preferred_element_type=jnp.float32)
    down_sum, _ = reduce_over_dp((second * scale).astype(jnp.bfloat16), replicas)
    hvp_tokens = jnp.dot(pick, returned, preferred_element_type=jnp.float32).astype(jnp.bfloat16)
    first = jnp.dot(tangent.T, back_pre, preferred_element_type=jnp.float32) + jnp.dot(
        primal.T, back_tan, preferred_element_type=jnp.float32
    )
    up_sum, hvp_tokens = reduce_over_dp(
        (first * scale).astype(jnp.bfloat16), replicas, hvp_tokens
    )
    hvp_up = up_sum[None]
    hvp_down = down_sum.T[None]
    return (hvp_tokens, hvp_up, hvp_down)


def solution(mesh):
    in_specs = (
        P(("dp", "expert"), None),
        P(("dp", "expert"), None),
        P(("dp", "expert"), None),
        P(("dp", "expert"), None),
        P(("dp", "expert"), None),
        P("expert", None, None),
        P("expert", None, None),
        P("expert", None, None),
    )
    out_specs = (P(("dp", "expert"), None), P("expert", "dp", None), P("expert", None, "dp"))
    return jax.shard_map(
        per_device, mesh=mesh, in_specs=in_specs, out_specs=out_specs, check_vma=False
    )
```

```python
import math

import jax
import jax.numpy as jnp
from jax import lax
from jax.sharding import PartitionSpec as P


def slot_matrices(route_ids, gate_rows, expert_count, capacity):
    token_count, route_count = route_ids.shape
    routes_total = token_count * route_count
    slots = expert_count * capacity
    flat_ids = route_ids.reshape(routes_total)
    onehot = (flat_ids[:, None] == jnp.arange(expert_count, dtype=jnp.int32)[None, :]).astype(
        jnp.bfloat16
    )
    order = jnp.arange(routes_total, dtype=jnp.int32)
    earlier = (order[None, :] < order[:, None]).astype(jnp.bfloat16)
    before = jnp.dot(earlier, onehot, preferred_element_type=jnp.float32)
    slot_rank = jnp.sum(before * onehot.astype(jnp.float32), axis=1).astype(jnp.int32)
    target = (flat_ids * capacity + slot_rank).reshape(token_count, route_count)
    slot_ids = jnp.arange(slots, dtype=jnp.int32)
    hit = target[:, :, None] == slot_ids[None, None, :]
    pick = jnp.any(hit, axis=1).astype(jnp.bfloat16)
    gate_slot = jnp.sum(jnp.where(hit, gate_rows.astype(jnp.float32)[:, :, None], 0.0), axis=(0, 1))
    return pick, gate_slot


def to_slots(pick, rows):
    return lax.dot_general(
        pick, rows, (((0,), (0,)), ((), ())), preferred_element_type=jnp.float32
    ).astype(jnp.bfloat16)


def reduce_over_dp(part, replicas, anchor=None):
    half = replicas // 2
    me = lax.axis_index("dp")
    core = me % 2
    row = me // 2
    blocks = part.reshape(half, 2, part.shape[0] // replicas, part.shape[1])
    keep = lax.dynamic_index_in_dim(blocks, core, axis=1, keepdims=False)
    give = lax.dynamic_index_in_dim(blocks, 1 - core, axis=1, keepdims=False)
    got = lax.ppermute(give, "dp", [(i, i ^ 1) for i in range(replicas)])
    partial = keep.astype(jnp.float32) + got.astype(jnp.float32)
    wire = partial.astype(jnp.bfloat16)
    wire = lax.dynamic_slice_in_dim(jnp.concatenate([wire, wire], 0), row, half, 0)
    received = []
    for step in range(1, half):
        pairs = [(i, (i + 2 * step) % replicas) for i in range(replicas)]
        received.append(lax.ppermute(wire[step], "dp", pairs))
    if anchor is not None:
        anchor, received = lax.optimization_barrier((anchor, received))
    total = lax.dynamic_index_in_dim(partial, row, axis=0, keepdims=False)
    for piece in received:
        total = total + piece.astype(jnp.float32)
    return total.astype(jnp.bfloat16), anchor


def per_device(tokens, tangents, cotangents, routes, gates, w_up, w_down, v_up):
    token_count, width = tokens.shape
    route_count = routes.shape[1]
    expert_count = lax.axis_size("expert")
    replicas = lax.axis_size("dp")
    capacity = max(2, token_count * route_count * 2 // expert_count)
    scale = 1.0 / math.sqrt(token_count * route_count * replicas)
    slots = expert_count * capacity
    pick, gate_slot = slot_matrices(routes, gates, expert_count, capacity)
    rows_xg = lax.dot_general(
        pick,
        jnp.concatenate([tokens, cotangents], axis=1),
        (((0,), (0,)), ((), ())),
        preferred_element_type=jnp.float32,
    )
    column = jnp.arange(2 * width, dtype=jnp.int32)[None, :]
    send_xg = (rows_xg * jnp.where(column < width, 1.0, gate_slot[:, None])).astype(jnp.bfloat16)
    send_tan = to_slots(pick, tangents)
    recv_xg = lax.all_to_all(
        send_xg.reshape(expert_count, capacity, 2 * width),
        "expert",
        split_axis=0,
        concat_axis=0,
        tiled=True,
    ).reshape(slots, 2 * width)
    recv_xg, send_tan = lax.optimization_barrier((recv_xg, send_tan))
    tangent = lax.all_to_all(
        send_tan.reshape(expert_count, capacity, width),
        "expert",
        split_axis=0,
        concat_axis=0,
        tiled=True,
    ).reshape(slots, width)
    primal = recv_xg[:, :width]
    scaled_cot = recv_xg[:, width:]
    up_proj = w_up[0]
    down_proj = w_down[0]
    dir_up = v_up[0]
    pre_act = jnp.dot(primal, up_proj, preferred_element_type=jnp.float32)
    sigmoid_z = jax.nn.sigmoid(pre_act)
    first_der = sigmoid_z * (1.0 + pre_act * (1.0 - sigmoid_z))
    second_der = sigmoid_z * (1.0 - sigmoid_z) * (2.0 + pre_act * (1.0 - 2.0 * sigmoid_z))
    back_hid = jnp.dot(scaled_cot, down_proj.T, preferred_element_type=jnp.float32)
    back_pre = (back_hid * first_der).astype(jnp.bfloat16)
    pre_mix = jnp.dot(primal, dir_up, preferred_element_type=jnp.float32)
    hvp_mix = jnp.dot(back_pre, dir_up.T, preferred_element_type=jnp.float32)
    pre_tan = jnp.dot(tangent, up_proj, preferred_element_type=jnp.float32) + pre_mix
    hidden_tan = (first_der * pre_tan).astype(jnp.bfloat16)
    back_tan = (back_hid * second_der * pre_tan).astype(jnp.bfloat16)
    input_hvp = (jnp.dot(back_tan, up_proj.T, preferred_element_type=jnp.float32) + hvp_mix).astype(
        jnp.bfloat16
    )
    first = jnp.dot(tangent.T, back_pre, preferred_element_type=jnp.float32) + jnp.dot(
        primal.T, back_tan, preferred_element_type=jnp.float32
    )
    up_part = (first * scale).astype(jnp.bfloat16)
    input_hvp, up_part, hidden_tan = lax.optimization_barrier((input_hvp, up_part, hidden_tan))
    returned = lax.all_to_all(
        input_hvp.reshape(expert_count, capacity, width),
        "expert",
        split_axis=0,
        concat_axis=0,
        tiled=True,
    ).reshape(slots, width)
    second = jnp.dot(scaled_cot.T, hidden_tan, preferred_element_type=jnp.float32)
    down_sum, _ = reduce_over_dp((second * scale).astype(jnp.bfloat16), replicas)
    hvp_tokens = jnp.dot(pick, returned, preferred_element_type=jnp.float32).astype(jnp.bfloat16)
    up_sum, hvp_tokens = reduce_over_dp(up_part, replicas, hvp_tokens)
    hvp_up = up_sum[None]
    hvp_down = down_sum.T[None]
    return (hvp_tokens, hvp_up, hvp_down)


def solution(mesh):
    in_specs = (
        P(("dp", "expert"), None),
        P(("dp", "expert"), None),
        P(("dp", "expert"), None),
        P(("dp", "expert"), None),
        P(("dp", "expert"), None),
        P("expert", None, None),
        P("expert", None, None),
        P("expert", None, None),
    )
    out_specs = (P(("dp", "expert"), None), P("expert", "dp", None), P("expert", None, "dp"))
    return jax.shard_map(
        per_device, mesh=mesh, in_specs=in_specs, out_specs=out_specs, check_vma=False
    )
```
